256 devices in a mesh: rep: 16 (over x_hi, z), fsdp: 16 (over x_lo, y, core).
Axes of the slice: x: 4 (x_hi: 2, x_lo: 2; x = x_hi * 2 + x_lo), y: 4, z: 8, core: 2. Of those that a mesh axis runs over, the one named last changes fastest.
Arguments:
- outer_start: float32 [2048, 8192], P(None, 'fsdp'), may hold values from -6 to 6
- local_weights: bfloat16 [16, 2048, 8192], P('rep', None, 'fsdp'), may hold values from -9 to 9
- momentum: float32 [2048, 8192], P('rep', 'fsdp'), may hold values from -0.6 to 0.6
Outputs:
- new_weights: bfloat16 [2048, 8192], P(None, 'fsdp')
- new_master: float32 [2048, 8192], P('rep', 'fsdp')
- new_momentum: float32 [2048, 8192], P('rep', 'fsdp')
The draws below stay inside these ranges and needn't reach their ends.
All inputs are finite; a program needn't handle non-finite values.
Results may differ from the reference program's by a relative error of at most 0.0045.
Values may be sent and summed in bfloat16 or wider, within the bound.
No kernel may reach another device: no remote copies, remote signals or barrier semaphores. Data moves between devices by JAX's collectives and lax.ppermute only.
A program may use at most 64 MiB of HBM per device.

```python
import math
import jax
import jax.numpy as jnp
from jax import lax

D = 8192
KV = 1024
REPLICAS = 16


def start_field(key):
    key_outer = jax.random.fold_in(key, 31)
    field = jax.random.truncated_normal(key_outer, -6.0, 6.0, (2 * KV, D), jnp.float32)
    return field


def draw_outer_start(key, part):
    return start_field(key)


def draw_local_weights(key, part):
    key_in, key_out, key_common, key_jitter = jax.random.split(jax.random.fold_in(key, 17), 4)
    column = jnp.arange(D, dtype=jnp.float32) / D
    in_scale = jnp.power(4.0, column) * jnp.exp(jax.random.uniform(key_in, (D,), jnp.float32, 0.0, math.log(2.5)))
    out_scale = jnp.exp(jax.random.uniform(key_out, (2 * KV,), jnp.float32, math.log(0.4), math.log(4.0)))
    drift_scale = 0.01
    common = 0.5 * jax.random.truncated_normal(key_common, -4.0, 4.0, (2 * KV, D), jnp.float32)
    jitter = jax.random.truncated_normal(key_jitter, -4.0, 4.0, (REPLICAS, 2 * KV, D), jnp.float32)
    scales = drift_scale * out_scale[:, None] * in_scale[None, :]
    drift_field = scales[None, :, :] * (common[None, :, :] + jitter)
    values = start_field(key)[None, :, :] + drift_field
    return values.astype(jnp.bfloat16)


def block_scale(key, dims, cuts, smallest, top_value):
    loudness = 1.0
    for axis_at, blocks in cuts:
        draws = jax.random.uniform(jax.random.fold_in(jax.random.fold_in(key, 6), axis_at), (blocks,), jnp.float32, smallest / len(cuts), top_value / len(cuts))
        loudness = loudness * jnp.repeat(jnp.exp(draws), dims[axis_at] // blocks).reshape((-1,) + (1,) * (len(dims) - 1 - axis_at))
    return loudness


def centred(key, dims, width, bound, cuts=(), kind=jnp.bfloat16):
    loudness = block_scale(key, dims, cuts, -0.22, 0.18) if cuts else 1.0
    entries = jax.random.normal(key, dims, jnp.float32) * width * loudness
    return jnp.minimum(jnp.maximum(entries, -bound), bound).astype(kind)


def setup_inputs(seed: int = 0) -> dict:
    key_list = jax.random.split(jax.random.key(seed), 4)
    outer_start = draw_outer_start(jax.random.fold_in(key_list[3], 71), 0)
    local_weights = draw_local_weights(jax.random.fold_in(key_list[3], 71), 0)
    momentum = centred(key_list[2], (2 * KV, D), 0.1, 0.6, ((0, 16), (1, 16)), jnp.float32)
    return {"outer_start": outer_start, "local_weights": local_weights, "momentum": momentum}


clip_level = 0.03
outer_rate = 0.7
momentum_coef = 0.9
eps_value = 1e-06

def reference(outer_start, local_weights, momentum):

    def add_replica(replica, summed):
        local_rows = local_weights[replica].astype(jnp.float32)
        rounded = (outer_start - local_rows).astype(jnp.bfloat16)
        rounded = lax.optimization_barrier(rounded)
        return summed + rounded.astype(jnp.float32)
    summed = lax.fori_loop(0, REPLICAS, add_replica, jnp.zeros(outer_start.shape, jnp.float32))
    outer_grad = summed / REPLICAS
    unit_squares = lax.optimization_barrier(jnp.sum(outer_grad * outer_grad, axis=1))
    factor = jnp.minimum(1.0, clip_level / jnp.sqrt(unit_squares / D + eps_value))
    clipped = outer_grad * factor[:, None]
    new_momentum = momentum_coef * momentum + clipped
    new_master = outer_start - outer_rate * (clipped + momentum_coef * new_momentum)
    return (new_master.astype(jnp.bfloat16), new_master, new_momentum)
```

```python
import jax
import jax.numpy as jnp
from jax import lax
from jax.sharding import PartitionSpec as P

D = 8192
clip_level = 0.03
outer_rate = 0.7
momentum_coef = 0.9
eps_value = 1e-06


def outer_update(own_outer, outer_grad, unit_squares, momentum_rows):
    factor = jnp.minimum(1.0, clip_level / jnp.sqrt(unit_squares / D + eps_value))
    clipped = outer_grad * factor[:, None]
    new_momentum = momentum_coef * momentum_rows + clipped
    new_master = own_outer - outer_rate * (clipped + momentum_coef * new_momentum)
    return (new_master, new_momentum)


def rs_psum_scatter(diff):
    return lax.psum_scatter(diff, "rep", scatter_dimension=0, tiled=True).astype(jnp.float32)


def rs_a2a(diff):
    n = lax.axis_size("rep")
    x = diff.reshape(n, diff.shape[0] // n, diff.shape[1])
    y = lax.all_to_all(x, "rep", 0, 0, tiled=False)
    return jnp.sum(y.astype(jnp.float32), axis=0)


def ag_all_gather(w):
    return lax.all_gather(w, "rep", axis=0, tiled=True)


def ag_a2a(w):
    n = lax.axis_size("rep")
    x = jnp.broadcast_to(w[None], (n,) + w.shape)
    y = lax.all_to_all(x, "rep", 0, 0, tiled=False)
    return y.reshape(n * w.shape[0], w.shape[1])


def sq_psum(s):
    return lax.psum(s, "fsdp")


def sq_a2a(s):
    n = lax.axis_size("fsdp")
    x = jnp.broadcast_to(s[None], (n,) + s.shape)
    y = lax.all_to_all(x, "fsdp", 0, 0, tiled=False)
    return jnp.sum(y, axis=0)


def sq_ag(s):
    return jnp.sum(lax.all_gather(s, "fsdp", axis=0, tiled=False), axis=0)


def make(rs, sq, ag):
    def on_device(outer_start, local_weights, momentum):
        local_shard = local_weights[0]
        replicas = lax.axis_size("rep")
        owner = lax.axis_index("rep")
        own_rows = outer_start.shape[0] // replicas
        diff = (outer_start - local_shard.astype(jnp.float32)).astype(jnp.bfloat16)
        summed = rs(diff)
        own_outer = lax.dynamic_slice_in_dim(outer_start, owner * own_rows, own_rows, 0)
        outer_grad = summed / replicas
        unit_squares = sq(jnp.sum(outer_grad * outer_grad, axis=1))
        new_master, new_momentum = outer_update(own_outer, outer_grad, unit_squares, momentum)
        new_weights = ag(new_master.astype(jnp.bfloat16))
        return (new_weights, new_master, new_momentum)

    def solution(mesh):
        return jax.shard_map(
            on_device,
            mesh=mesh,
            in_specs=(P(None, "fsdp"), P("rep", None, "fsdp"), P("rep", "fsdp")),
            out_specs=(P(None, "fsdp"), P("rep", "fsdp"), P("rep", "fsdp")),
            check_vma=False,
        )
    return solution
solution = make(rs_a2a, sq_a2a, ag_a2a)
```

```python
import jax
import jax.numpy as jnp
from jax import lax
from jax.sharding import PartitionSpec as P

D = 8192
clip_level = 0.03
outer_rate = 0.7
momentum_coef = 0.9
eps_value = 1e-06


def outer_update(own_outer, outer_grad, unit_squares, momentum_rows):
    factor = jnp.minimum(1.0, clip_level / jnp.sqrt(unit_squares / D + eps_value))
    clipped = outer_grad * factor[:, None]
    new_momentum = momentum_coef * momentum_rows + clipped
    new_master = own_outer - outer_rate * (clipped + momentum_coef * new_momentum)
    return (new_master, new_momentum)


def rs_psum_scatter(diff):
    return lax.psum_scatter(diff, "rep", scatter_dimension=0, tiled=True).astype(jnp.float32)


def rs_a2a(diff):
    n = lax.axis_size("rep")
    x = diff.reshape(n, diff.shape[0] // n, diff.shape[1])
    y = lax.all_to_all(x, "rep", 0, 0, tiled=False)
    return jnp.sum(y.astype(jnp.float32), axis=0)


def ag_all_gather(w):
    return lax.all_gather(w, "rep", axis=0, tiled=True)


def ag_a2a(w):
    n = lax.axis_size("rep")
    x = jnp.broadcast_to(w[None], (n,) + w.shape)
    y = lax.all_to_all(x, "rep", 0, 0, tiled=False)
    return y.reshape(n * w.shape[0], w.shape[1])


def sq_psum(s):
    return lax.psum(s, "fsdp")


def sq_a2a(s):
    n = lax.axis_size("fsdp")
    x = jnp.broadcast_to(s[None], (n,) + s.shape)
    y = lax.all_to_all(x, "fsdp", 0, 0, tiled=False)
    return jnp.sum(y, axis=0)


def sq_ag(s):
    return jnp.sum(lax.all_gather(s, "fsdp", axis=0, tiled=False), axis=0)


def make(rs, sq, ag):
    def on_device(outer_start, local_weights, momentum):
        local_shard = local_weights[0]
        replicas = lax.axis_size("rep")
        owner = lax.axis_index("rep")
        own_rows = outer_start.shape[0] // replicas
        diff = (outer_start - local_shard.astype(jnp.float32)).astype(jnp.bfloat16)
        summed = rs(diff)
        own_outer = lax.dynamic_slice_in_dim(outer_start, owner * own_rows, own_rows, 0)
        outer_grad = summed / replicas
        unit_squares = sq(jnp.sum(outer_grad * outer_grad, axis=1))
        new_master, new_momentum = outer_update(own_outer, outer_grad, unit_squares, momentum)
        new_weights = ag(new_master.astype(jnp.bfloat16))
        return (new_weights, new_master, new_momentum)

    def solution(mesh):
        return jax.shard_map(
            on_device,
            mesh=mesh,
            in_specs=(P(None, "fsdp"), P("rep", None, "fsdp"), P("rep", "fsdp")),
            out_specs=(P(None, "fsdp"), P("rep", "fsdp"), P("rep", "fsdp")),
            check_vma=False,
        )
    return solution

NX = 2


def _perms(n):
    nz = n // NX
    cw = [(x * nz + k, x * nz + (k + 1) % nz) for x in range(NX) for k in range(nz)]
    ccw = [(x * nz + k, x * nz + (k - 1) % nz) for x in range(NX) for k in range(nz)]
    xp = [(x * nz + k, (1 - x) * nz + k) for x in range(NX) for k in range(nz)]
    return nz, cw, ccw, xp


def rs_ring4(diff):
    n = lax.axis_size("rep")
    nz, cw, ccw, xp = _perms(n)
    r = lax.axis_index("rep")
    xh, z = r // nz, r % nz
    rows = diff.shape[0] // n
    t = diff.reshape(NX, nz, rows, diff.shape[1])
    take = lambda i: lax.dynamic_index_in_dim(t, i % nz, 1, keepdims=False)
    n_cw, n_ccw = nz // 2, (nz - 1) // 2
    send_cw, send_ccw = take(z + n_cw), take(z - n_ccw)
    for s in range(n_cw):
        got_cw = lax.ppermute(send_cw, "rep", cw)
        if s < n_ccw:
            got_ccw = lax.ppermute(send_ccw, "rep", ccw)
        if s < n_cw - 1:
            send_cw = (got_cw.astype(jnp.float32) + take(z + n_cw - 1 - s).astype(jnp.float32)).astype(jnp.bfloat16)
        if s < n_ccw - 1:
            send_ccw = (got_ccw.astype(jnp.float32) + take(z - n_ccw + 1 + s).astype(jnp.float32)).astype(jnp.bfloat16)
    own = take(z).astype(jnp.float32) + got_cw.astype(jnp.float32) + got_ccw.astype(jnp.float32)
    first = xh == 0
    mine = jnp.where(first, own[0], own[1])
    other = jnp.where(first, own[1], own[0]).astype(jnp.bfloat16)
    return mine + lax.ppermute(other, "rep", xp).astype(jnp.float32)


def ag_ring4(w):
    n = lax.axis_size("rep")
    nz, cw, ccw, xp = _perms(n)
    r = lax.axis_index("rep")
    xh, z = r // nz, r % nz
    wx = lax.ppermute(w, "rep", xp)
    first = xh == 0
    blk = jnp.stack([jnp.where(first, w, wx), jnp.where(first, wx, w)])
    n_cw, n_ccw = nz // 2, (nz - 1) // 2
    cur_cw, cur_ccw = blk, blk
    got_cw, got_ccw = [], []
    for s in range(n_cw):
        cur_cw = lax.ppermute(cur_cw, "rep", cw)
        got_cw.append(cur_cw)
        if s < n_ccw:
            cur_ccw = lax.ppermute(cur_ccw, "rep", ccw)
            got_ccw.append(cur_ccw)
    by_offset = [blk] + got_ccw + got_cw[::-1]
    stacked = jnp.stack(by_offset, axis=1)
    out = jnp.roll(stacked, z, axis=1)
    return out.reshape(n * w.shape[0], w.shape[1])
solution = make(rs_ring4, sq_a2a, ag_ring4)
```

```python
import jax
import jax.numpy as jnp
from jax import lax
from jax.sharding import PartitionSpec as P

D = 8192
NX = 2

clip_level = 0.03
outer_rate = 0.7
momentum_coef = 0.9
eps_value = 1e-06


def outer_update(own_outer, outer_grad, unit_squares, momentum_rows):
    factor = jnp.minimum(1.0, clip_level / jnp.sqrt(unit_squares / D + eps_value))
    clipped = outer_grad * factor[:, None]
    new_momentum = momentum_coef * momentum_rows + clipped
    new_master = own_outer - outer_rate * (clipped + momentum_coef * new_momentum)
    return (new_master, new_momentum)


def ring_perms(n):
    nz = n // NX
    cw = [(x * nz + k, x * nz + (k + 1) % nz) for x in range(NX) for k in range(nz)]
    ccw = [(x * nz + k, x * nz + (k - 1) % nz) for x in range(NX) for k in range(nz)]
    xp = [(x * nz + k, (1 - x) * nz + k) for x in range(NX) for k in range(nz)]
    return nz, cw, ccw, xp


def f32(x):
    return x.astype(jnp.float32)


def reduce_scatter(term, n):
    nz, cw, ccw, xp = ring_perms(n)
    r = lax.axis_index("rep")
    xh, z = r // nz, r % nz
    steps = nz // 2
    half = term(z).shape[-1] // 2
    send_cw = term(z + steps)[..., :half]
    send_ccw = term(z - steps)[..., half:]
    for s in range(steps):
        got_cw = lax.ppermute(send_cw, "rep", cw)
        got_ccw = lax.ppermute(send_ccw, "rep", ccw)
        if s == steps - 1:
            break
        own_cw = f32(term(z + steps - 1 - s))
        own_ccw = f32(term(z - steps + 1 + s))
        if s == 0:
            send_cw = jnp.concatenate([f32(got_cw) + own_cw[..., :half], own_cw[..., half:]], axis=-1)
            send_ccw = jnp.concatenate([own_ccw[..., :half], f32(got_ccw) + own_ccw[..., half:]], axis=-1)
        else:
            send_cw = f32(got_cw) + own_cw
            send_ccw = f32(got_ccw) + own_ccw
        send_cw = send_cw.astype(jnp.bfloat16)
        send_ccw = send_ccw.astype(jnp.bfloat16)
    total = (f32(term(z)) + f32(got_cw) + f32(got_ccw)).astype(jnp.bfloat16)
    return f32(total) + f32(lax.ppermute(total, "rep", xp))


def all_gather(w, n):
    nz, cw, ccw, xp = ring_perms(n)
    r = lax.axis_index("rep")
    xh, z = r // nz, r % nz
    blk = w
    rows, cols = w.shape[1:]
    half = cols // 2
    out = jnp.zeros((NX, nz, rows, cols), w.dtype)
    put = lambda o, piece, pos, col: lax.dynamic_update_slice(o, piece[:, None], (0, pos % nz, 0, col))
    out = put(out, blk, z, 0)
    steps = nz // 2
    cur_cw, cur_ccw = blk, blk
    for s in range(steps):
        if s == steps - 1:
            cur_cw = cur_cw[..., :half]
            cur_ccw = cur_ccw[..., half:]
        cur_cw = lax.ppermute(cur_cw, "rep", cw)
        cur_ccw = lax.ppermute(cur_ccw, "rep", ccw)
        out = put(out, cur_cw, z - 1 - s, 0)
        out = put(out, cur_ccw, z + 1 + s, half if s == steps - 1 else 0)
    return out.reshape(n * rows, cols)


def on_device(outer_start, local_weights, momentum):
    local_shard = local_weights[0]
    replicas = lax.axis_size("rep")
    owner = lax.axis_index("rep")
    own_rows = outer_start.shape[0] // replicas
    cols = outer_start.shape[1]
    nz = replicas // NX
    start_blocks = outer_start.reshape(NX, nz, own_rows, cols)
    local_blocks = local_shard.reshape(NX, nz, own_rows, cols)

    def term(i):
        i = i % nz
        a = lax.dynamic_index_in_dim(start_blocks, i, 1, keepdims=False)
        b = lax.dynamic_index_in_dim(local_blocks, i, 1, keepdims=False)
        return (a - b.astype(jnp.float32)).astype(jnp.bfloat16)

    xh = owner // nz
    first = xh == 0
    partner_momentum = lax.ppermute(momentum, "rep", ring_perms(replicas)[3])
    both_momentum = jnp.stack([jnp.where(first, momentum, partner_momentum), jnp.where(first, partner_momentum, momentum)])
    summed = reduce_scatter(term, replicas)
    both_outer = lax.dynamic_index_in_dim(start_blocks, owner % nz, 1, keepdims=False)
    outer_grad = summed / replicas
    partial = jnp.sum(outer_grad * outer_grad, axis=2)
    shards = lax.axis_size("fsdp")
    spread = jnp.broadcast_to(partial[None], (shards,) + partial.shape)
    unit_squares = jnp.sum(lax.all_to_all(spread, "fsdp", 0, 0, tiled=False), axis=0)
    factor = jnp.minimum(1.0, clip_level / jnp.sqrt(unit_squares / D + eps_value))
    clipped = outer_grad * factor[..., None]
    both_new_momentum = momentum_coef * both_momentum + clipped
    both_new_master = both_outer - outer_rate * (clipped + momentum_coef * both_new_momentum)
    new_weights = all_gather(both_new_master.astype(jnp.bfloat16), replicas)
    new_master = lax.dynamic_index_in_dim(both_new_master, xh, 0, keepdims=False)
    new_momentum = lax.dynamic_index_in_dim(both_new_momentum, xh, 0, keepdims=False)
    return (new_weights, new_master, new_momentum)


def solution(mesh):
    return jax.shard_map(
        on_device,
        mesh=mesh,
        in_specs=(P(None, "fsdp"), P("rep", None, "fsdp"), P("rep", "fsdp")),
        out_specs=(P(None, "fsdp"), P("rep", "fsdp"), P("rep", "fsdp")),
        check_vma=False,
    )
```

```python
import jax
import jax.numpy as jnp
from jax import lax
from jax.sharding import PartitionSpec as P

D = 8192
NX = 2

clip_level = 0.03
outer_rate = 0.7
momentum_coef = 0.9
eps_value = 1e-06


def outer_update(own_outer, outer_grad, unit_squares, momentum_rows):
    factor = jnp.minimum(1.0, clip_level / jnp.sqrt(unit_squares / D + eps_value))
    clipped = outer_grad * factor[:, None]
    new_momentum = momentum_coef * momentum_rows + clipped
    new_master = own_outer - outer_rate * (clipped + momentum_coef * new_momentum)
    return (new_master, new_momentum)


def ring_perms(n):
    nz = n // NX
    cw = [(x * nz + k, x * nz + (k + 1) % nz) for x in range(NX) for k in range(nz)]
    ccw = [(x * nz + k, x * nz + (k - 1) % nz) for x in range(NX) for k in range(nz)]
    xp = [(x * nz + k, (1 - x) * nz + k) for x in range(NX) for k in range(nz)]
    return nz, cw, ccw, xp


def f32(x):
    return x.astype(jnp.float32)


def reduce_scatter(term, n):
    nz, cw, ccw, xp = ring_perms(n)
    r = lax.axis_index("rep")
    xh, z = r // nz, r % nz
    steps = nz // 2
    half = term(z).shape[-1] // 2
    send_cw, send_ccw = lax.optimization_barrier((term(z + steps)[..., :half], term(z - steps)[..., half:]))
    for s in range(steps):
        got_cw = lax.ppermute(send_cw, "rep", cw)
        got_ccw = lax.ppermute(send_ccw, "rep", ccw)
        if s == steps - 1:
            break
        own_cw, own_ccw = lax.optimization_barrier((term(z + steps - 1 - s), term(z - steps + 1 + s)))
        own_cw, own_ccw = f32(own_cw), f32(own_ccw)
        if s == 0:
            send_cw = jnp.concatenate([f32(got_cw) + own_cw[..., :half], own_cw[..., half:]], axis=-1)
            send_ccw = jnp.concatenate([own_ccw[..., :half], f32(got_ccw) + own_ccw[..., half:]], axis=-1)
        else:
            send_cw = f32(got_cw) + own_cw
            send_ccw = f32(got_ccw) + own_ccw
        send_cw = send_cw.astype(jnp.bfloat16)
        send_ccw = send_ccw.astype(jnp.bfloat16)
    own = lax.optimization_barrier(term(z))
    total = (f32(own) + f32(got_cw) + f32(got_ccw)).astype(jnp.bfloat16)
    return f32(total) + f32(lax.ppermute(total, "rep", xp))


def all_gather(w, n):
    nz, cw, ccw, xp = ring_perms(n)
    r = lax.axis_index("rep")
    xh, z = r // nz, r % nz
    blk = w
    rows, cols = w.shape[1:]
    half = cols // 2
    out = jnp.zeros((NX, nz, rows, cols), w.dtype)
    put = lambda o, piece, pos, col: lax.dynamic_update_slice(o, piece[:, None], (0, pos % nz, 0, col))
    out = put(out, blk, z, 0)
    steps = nz // 2
    cur_cw, cur_ccw = blk, blk
    for s in range(steps):
        if s == steps - 1:
            cur_cw = cur_cw[..., :half]
            cur_ccw = cur_ccw[..., half:]
        cur_cw = lax.ppermute(cur_cw, "rep", cw)
        cur_ccw = lax.ppermute(cur_ccw, "rep", ccw)
        out = put(out, cur_cw, z - 1 - s, 0)
        out = put(out, cur_ccw, z + 1 + s, half if s == steps - 1 else 0)
    return out.reshape(n * rows, cols)


def on_device(outer_start, local_weights, momentum):
    local_shard = local_weights[0]
    replicas = lax.axis_size("rep")
    owner = lax.axis_index("rep")
    own_rows = outer_start.shape[0] // replicas
    cols = outer_start.shape[1]
    nz = replicas // NX
    start_blocks = outer_start.reshape(NX, nz, own_rows, cols)
    local_blocks = local_shard.reshape(NX, nz, own_rows, cols)

    def term(i):
        i = i % nz
        a = lax.dynamic_index_in_dim(start_blocks, i, 1, keepdims=False)
        b = lax.dynamic_index_in_dim(local_blocks, i, 1, keepdims=False)
        return (a - b.astype(jnp.float32)).astype(jnp.bfloat16)

    xh = owner // nz
    first = xh == 0
    partner_momentum = lax.ppermute(momentum, "rep", ring_perms(replicas)[3])
    both_momentum = jnp.stack([jnp.where(first, momentum, partner_momentum), jnp.where(first, partner_momentum, momentum)])
    summed = reduce_scatter(term, replicas)
    both_outer = lax.dynamic_index_in_dim(start_blocks, owner % nz, 1, keepdims=False)
    outer_grad = summed / replicas
    partial = jnp.sum(outer_grad * outer_grad, axis=2)
    shards = lax.axis_size("fsdp")
    spread = jnp.broadcast_to(partial[None], (shards,) + partial.shape)
    unit_squares = jnp.sum(lax.all_to_all(spread, "fsdp", 0, 0, tiled=False), axis=0)
    factor = jnp.minimum(1.0, clip_level / jnp.sqrt(unit_squares / D + eps_value))
    clipped = outer_grad * factor[..., None]
    both_new_momentum = momentum_coef * both_momentum + clipped
    both_new_master = both_outer - outer_rate * (clipped + momentum_coef * both_new_momentum)
    new_weights = all_gather(both_new_master.astype(jnp.bfloat16), replicas)
    new_master = lax.dynamic_index_in_dim(both_new_master, xh, 0, keepdims=False)
    new_momentum = lax.dynamic_index_in_dim(both_new_momentum, xh, 0, keepdims=False)
    return (new_weights, new_master, new_momentum)


def solution(mesh):
    return jax.shard_map(
        on_device,
        mesh=mesh,
        in_specs=(P(None, "fsdp"), P("rep", None, "fsdp"), P("rep", "fsdp")),
        out_specs=(P(None, "fsdp"), P("rep", "fsdp"), P("rep", "fsdp")),
        check_vma=False,
    )
```

```python
import jax
import jax.numpy as jnp
from jax import lax
from jax.sharding import PartitionSpec as P

D = 8192
NX = 2

clip_level = 0.03
outer_rate = 0.7
momentum_coef = 0.9
eps_value = 1e-06


def outer_update(own_outer, outer_grad, unit_squares, momentum_rows):
    factor = jnp.minimum(1.0, clip_level / jnp.sqrt(unit_squares / D + eps_value))
    clipped = outer_grad * factor[:, None]
    new_momentum = momentum_coef * momentum_rows + clipped
    new_master = own_outer - outer_rate * (clipped + momentum_coef * new_momentum)
    return (new_master, new_momentum)


def ring_perms(n):
    nz = n // NX
    cw = [(x * nz + k, x * nz + (k + 1) % nz) for x in range(NX) for k in range(nz)]
    ccw = [(x * nz + k, x * nz + (k - 1) % nz) for x in range(NX) for k in range(nz)]
    xp = [(x * nz + k, (1 - x) * nz + k) for x in range(NX) for k in range(nz)]
    return nz, cw, ccw, xp


def f32(x):
    return x.astype(jnp.float32)


def reduce_scatter(term, n):
    nz, cw, ccw, xp = ring_perms(n)
    r = lax.axis_index("rep")
    xh, z = r // nz, r % nz
    steps = nz // 2
    send_cw, send_ccw = lax.optimization_barrier((term(z + steps)[:1], term(z - steps)[1:]))
    for s in range(steps):
        got_cw = lax.ppermute(send_cw, "rep", cw)
        got_ccw = lax.ppermute(send_ccw, "rep", ccw)
        if s == steps - 1:
            break
        own_cw, own_ccw = lax.optimization_barrier((term(z + steps - 1 - s), term(z - steps + 1 + s)))
        own_cw, own_ccw = f32(own_cw), f32(own_ccw)
        if s == 0:
            send_cw = jnp.concatenate([f32(got_cw) + own_cw[:1], own_cw[1:]])
            send_ccw = jnp.concatenate([own_ccw[:1], f32(got_ccw) + own_ccw[1:]])
        else:
            send_cw = f32(got_cw) + own_cw
            send_ccw = f32(got_ccw) + own_ccw
        send_cw = send_cw.astype(jnp.bfloat16)
        send_ccw = send_ccw.astype(jnp.bfloat16)
    own = lax.optimization_barrier(term(z))
    total = (f32(own) + f32(got_cw) + f32(got_ccw)).astype(jnp.bfloat16)
    return f32(total) + f32(lax.ppermute(total, "rep", xp))


def all_gather(w, n):
    nz, cw, ccw, xp = ring_perms(n)
    r = lax.axis_index("rep")
    xh, z = r // nz, r % nz
    blk = w
    rows, cols = w.shape[1:]
    out = jnp.zeros((NX, nz, rows, cols), w.dtype)
    put = lambda o, piece, pos, row: lax.dynamic_update_slice(o, piece[:, None], (row, pos % nz, 0, 0))
    out = put(out, blk, z, 0)
    steps = nz // 2
    cur_cw, cur_ccw = blk, blk
    for s in range(steps):
        if s == steps - 1:
            cur_cw = cur_cw[:1]
            cur_ccw = cur_ccw[1:]
        cur_cw = lax.ppermute(cur_cw, "rep", cw)
        cur_ccw = lax.ppermute(cur_ccw, "rep", ccw)
        out = put(out, cur_cw, z - 1 - s, 0)
        out = put(out, cur_ccw, z + 1 + s, 1 if s == steps - 1 else 0)
    return out.reshape(n * rows, cols)


def on_device(outer_start, local_weights, momentum):
    local_shard = local_weights[0]
    replicas = lax.axis_size("rep")
    owner = lax.axis_index("rep")
    own_rows = outer_start.shape[0] // replicas
    cols = outer_start.shape[1]
    nz = replicas // NX
    start_blocks = outer_start.reshape(NX, nz, own_rows, cols)
    local_blocks = local_shard.reshape(NX, nz, own_rows, cols)

    def term(i):
        i = i % nz
        a = lax.dynamic_index_in_dim(start_blocks, i, 1, keepdims=False)
        b = lax.dynamic_index_in_dim(local_blocks, i, 1, keepdims=False)
        return (a - b.astype(jnp.float32)).astype(jnp.bfloat16)

    xh = owner // nz
    first = xh == 0
    partner_momentum = lax.ppermute(momentum, "rep", ring_perms(replicas)[3])
    both_momentum = jnp.stack([jnp.where(first, momentum, partner_momentum), jnp.where(first, partner_momentum, momentum)])
    summed = reduce_scatter(term, replicas)
    both_outer = lax.dynamic_index_in_dim(start_blocks, owner % nz, 1, keepdims=False)
    outer_grad = summed / replicas
    partial = jnp.sum(outer_grad * outer_grad, axis=2)
    shards = lax.axis_size("fsdp")
    spread = jnp.broadcast_to(partial[None], (shards,) + partial.shape)
    unit_squares = jnp.sum(lax.all_to_all(spread, "fsdp", 0, 0, tiled=False), axis=0)
    factor = jnp.minimum(1.0, clip_level / jnp.sqrt(unit_squares / D + eps_value))
    clipped = outer_grad * factor[..., None]
    both_new_momentum = momentum_coef * both_momentum + clipped
    both_new_master = both_outer - outer_rate * (clipped + momentum_coef * both_new_momentum)
    new_weights = all_gather(both_new_master.astype(jnp.bfloat16), replicas)
    new_master = lax.dynamic_index_in_dim(both_new_master, xh, 0, keepdims=False)
    new_momentum = lax.dynamic_index_in_dim(both_new_momentum, xh, 0, keepdims=False)
    return (new_weights, new_master, new_momentum)


def solution(mesh):
    return jax.shard_map(
        on_device,
        mesh=mesh,
        in_specs=(P(None, "fsdp"), P("rep", None, "fsdp"), P("rep", "fsdp")),
        out_specs=(P(None, "fsdp"), P("rep", "fsdp"), P("rep", "fsdp")),
        check_vma=False,
    )
```

```python
import jax
import jax.numpy as jnp
from jax import lax
from jax.sharding import PartitionSpec as P

D = 8192
NX = 2

clip_level = 0.03
outer_rate = 0.7
momentum_coef = 0.9
eps_value = 1e-06


def outer_update(own_outer, outer_grad, unit_squares, momentum_rows):
    factor = jnp.minimum(1.0, clip_level / jnp.sqrt(unit_squares / D + eps_value))
    clipped = outer_grad * factor[:, None]
    new_momentum = momentum_coef * momentum_rows + clipped
    new_master = own_outer - outer_rate * (clipped + momentum_coef * new_momentum)
    return (new_master, new_momentum)


def ring_perms(n):
    nz = n // NX
    cw = [(x * nz + k, x * nz + (k + 1) % nz) for x in range(NX) for k in range(nz)]
    ccw = [(x * nz + k, x * nz + (k - 1) % nz) for x in range(NX) for k in range(nz)]
    xp = [(x * nz + k, (1 - x) * nz + k) for x in range(NX) for k in range(nz)]
    return nz, cw, ccw, xp


def f32(x):
    return x.astype(jnp.float32)


def reduce_scatter(term, n):
    nz, cw, ccw, xp = ring_perms(n)
    r = lax.axis_index("rep")
    xh, z = r // nz, r % nz
    steps = nz // 2
    send_cw, send_ccw = lax.optimization_barrier((term(z + steps)[:1], term(z - steps)[1:]))
    for s in range(steps):
        got_cw = lax.ppermute(send_cw, "rep", cw)
        got_ccw = lax.ppermute(send_ccw, "rep", ccw)
        if s == steps - 1:
            break
        own_cw, own_ccw = lax.optimization_barrier((term(z + steps - 1 - s), term(z - steps + 1 + s)))
        own_cw, own_ccw = f32(own_cw), f32(own_ccw)
        if s == 0:
            send_cw = jnp.concatenate([f32(got_cw) + own_cw[:1], own_cw[1:]])
            send_ccw = jnp.concatenate([own_ccw[:1], f32(got_ccw) + own_ccw[1:]])
        else:
            send_cw = f32(got_cw) + own_cw
            send_ccw = f32(got_ccw) + own_ccw
        send_cw = send_cw.astype(jnp.bfloat16)
        send_ccw = send_ccw.astype(jnp.bfloat16)
    own = lax.optimization_barrier(term(z))
    total = (f32(own) + f32(got_cw) + f32(got_ccw)).astype(jnp.bfloat16)
    return f32(total) + f32(lax.ppermute(total, "rep", xp))


def all_gather(w, n):
    nz, cw, ccw, xp = ring_perms(n)
    r = lax.axis_index("rep")
    xh, z = r // nz, r % nz
    blk = w
    rows, cols = w.shape[1:]
    out = jnp.zeros((NX, nz, rows, cols), w.dtype)
    put = lambda o, piece, pos, row: lax.dynamic_update_slice(o, piece[:, None], (row, pos % nz, 0, 0))
    out = put(out, blk, z, 0)
    steps = nz // 2
    cur_cw, cur_ccw = blk, blk
    for s in range(steps):
        if s == steps - 1:
            cur_cw = cur_cw[:1]
            cur_ccw = cur_ccw[1:]
        cur_cw = lax.ppermute(cur_cw, "rep", cw)
        cur_ccw = lax.ppermute(cur_ccw, "rep", ccw)
        out = put(out, cur_cw, z - 1 - s, 0)
        out = put(out, cur_ccw, z + 1 + s, 1 if s == steps - 1 else 0)
    return out.reshape(n * rows, cols)


def on_device(outer_start, local_weights, momentum):
    local_shard = local_weights[0]
    replicas = lax.axis_size("rep")
    owner = lax.axis_index("rep")
    own_rows = outer_start.shape[0] // replicas
    cols = outer_start.shape[1]
    nz = replicas // NX
    start_blocks = outer_start.reshape(NX, nz, own_rows, cols)
    local_blocks = local_shard.reshape(NX, nz, own_rows, cols)

    def term(i):
        i = i % nz
        a = lax.dynamic_index_in_dim(start_blocks, i, 1, keepdims=False)
        b = lax.dynamic_index_in_dim(local_blocks, i, 1, keepdims=False)
        return (a - b.astype(jnp.float32)).astype(jnp.bfloat16)

    xh = owner // nz
    first = xh == 0
    partner_momentum = lax.ppermute(momentum, "rep", ring_perms(replicas)[3])
    both_momentum = jnp.stack([jnp.where(first, momentum, partner_momentum), jnp.where(first, partner_momentum, momentum)])
    summed = reduce_scatter(term, replicas)
    both_outer = lax.dynamic_index_in_dim(start_blocks, owner % nz, 1, keepdims=False)
    outer_grad = summed / replicas
    partial = jnp.sum(outer_grad * outer_grad, axis=2)
    shards = lax.axis_size("fsdp")
    spread = jnp.broadcast_to(partial[None], (shards,) + partial.shape)
    unit_squares = jnp.sum(lax.all_to_all(spread, "fsdp", 0, 0, tiled=False), axis=0)
    factor = jnp.minimum(1.0, clip_level / jnp.sqrt(unit_squares / D + eps_value))
    clipped = outer_grad * factor[..., None]
    both_new_momentum = momentum_coef * both_momentum + clipped
    both_new_master = both_outer - outer_rate * (clipped + momentum_coef * both_new_momentum)
    new_weights = all_gather(lax.optimization_barrier(both_new_master.astype(jnp.bfloat16)), replicas)
    new_master = lax.dynamic_index_in_dim(both_new_master, xh, 0, keepdims=False)
    new_momentum = lax.dynamic_index_in_dim(both_new_momentum, xh, 0, keepdims=False)
    return (new_weights, new_master, new_momentum)


def solution(mesh):
    return jax.shard_map(
        on_device,
        mesh=mesh,
        in_specs=(P(None, "fsdp"), P("rep", None, "fsdp"), P("rep", "fsdp")),
        out_specs=(P(None, "fsdp"), P("rep", "fsdp"), P("rep", "fsdp")),
        check_vma=False,
    )
```
